512 devices in a mesh: phase: 16 (over x, z_hi), slab: 32 (over z_lo, y, core).
Axes of the slice: x: 4, y: 4, z: 16 (z_hi: 4, z_lo: 4; z = z_hi * 4 + z_lo), core: 2. Of those that a mesh axis runs over, the one named last changes fastest.
Arguments:
- pressure: float32 [2, 64, 32, 98304], P(None, 'phase', None, 'slab'), may hold values from -6 to 6
- mode_shapes: float32 [1024, 98304], P('phase', 'slab'), may hold values from -0.0390625 to 0.0390625
- point_weight: float32 [98304], P('slab'), may hold values from 0.5 to 2
- panel_order: int32 [8], replicated, may hold values from 0 to 7, each once
Outputs:
- influence: float32 [2, 64, 32, 1024], P(None, None, 'phase', 'slab')
The draws below stay inside these ranges and needn't reach their ends.
Inputs may be any that keep to these rules, and one draw needn't show every extreme that they name: panel_order names each of 0 to 7 once.
All inputs are finite; a program needn't handle non-finite values.
Results may differ from the reference program's by a relative error of at most 0.00007.
Values sent between devices are 32-bit elements; how exact they have to be, the bound alone decides.
No kernel may reach another device: no remote copies, remote signals or barrier semaphores. Data moves between devices by JAX's collectives and lax.ppermute only.
A program may use at most 64 MiB of HBM per device.

```python
import math
import jax
import jax.numpy as jnp
from jax import lax

NB = 64
J = 32
S = 98304
MODES = 1024
PANEL = 128
NPANEL = 8


def raised(array, rng, source, target, blocks, factor):
    def block_of(axis_at):
        return (jnp.arange(array.shape[axis_at]) // (array.shape[axis_at] // blocks)).reshape((-1,) + (1,) * (array.ndim - 1 - axis_at))

    near = jax.random.permutation(rng, blocks)[block_of(target)]
    far = (block_of(target) + blocks // 2) % blocks
    return jnp.where((block_of(source) == near) | (block_of(source) == far), factor * array, array)


def levels(stream_key, shape, split, low, largest):
    def one(axis_at, blocks):
        heights = jax.random.uniform(jax.random.fold_in(jax.random.fold_in(stream_key, 6), axis_at), (blocks,), jnp.float32, low / len(split), largest / len(split))
        return jnp.repeat(jnp.exp(heights), shape[axis_at] // blocks).reshape((-1,) + (1,) * (len(shape) - axis_at - 1))

    gain = one(*split[0])
    for cut in split[1:]:
        gain = gain * one(*cut)
    return gain


def centred(stream_key, shape, scale, reach, cuts=(), held_as=jnp.bfloat16):
    array = scale * jax.random.normal(stream_key, shape, jnp.float32)
    if cuts:
        array = array * levels(stream_key, shape, cuts, -0.22, 0.18)
    return jnp.clip(array, -reach, reach).astype(held_as)


def noise_with(stream_key, dims, width, limit, pieces, heavy, held_as=jnp.bfloat16):
    drawn = width * jax.random.normal(stream_key, dims, jnp.float32)
    if pieces:
        drawn = drawn * levels(stream_key, dims, pieces, -0.22, 0.18)
    return jnp.clip(raised(drawn, jax.random.fold_in(stream_key, 3), *heavy), -limit, limit).astype(held_as)


def setup_inputs(seed: int = 0) -> dict:
    key_list = jax.random.split(jax.random.key(seed), 5)
    pressure = centred(key_list[0], (2, NB, J, S), 1.0, 6.0, ((1, 16), (3, 32)), jnp.float32)
    mode_shapes = noise_with(key_list[1], (MODES, S), S ** -0.5, 0.0390625, ((0, 16), (1, 32)), (1, 0, 32, 2.75), jnp.float32)
    point_weight = jnp.clip(jnp.exp(math.log(2.0) - 1.3862944 * jax.random.uniform(key_list[2], (S,), jnp.float32) ** levels(key_list[2], (S,), ((0, 32),), -0.2, 0.2)), 0.5, 2.0)
    panel_order = jax.random.permutation(key_list[3], NPANEL).astype(jnp.int32)
    return {"pressure": pressure, "mode_shapes": mode_shapes, "point_weight": point_weight, "panel_order": panel_order}


def blade_table(blades):
    phases = jnp.arange(blades, dtype=jnp.int32)
    index = phases[None, :] * phases[:, None] % blades
    theta = index.astype(jnp.float32) * (2.0 * math.pi / blades)
    cosine = jnp.cos(theta)
    sine = jnp.sin(theta)
    upper = jnp.concatenate([cosine, -sine], axis=1)
    lower = jnp.concatenate([sine, cosine], axis=1)
    return jnp.concatenate([upper, lower], axis=0) * (1.0 / math.sqrt(blades))

def reference(pressure, mode_shapes, point_weight, panel_order):
    weighted = mode_shapes * point_weight[None, :]
    rows = pressure.reshape(2 * NB * J, S)
    forces = lax.dot_general(rows, weighted, (((1,), (1,)), ((), ())), precision=lax.Precision.HIGHEST, preferred_element_type=jnp.float32)
    panels = forces.reshape(2 * NB * J, NPANEL, PANEL)
    reordered = jnp.take(panels, panel_order.astype(jnp.int32), axis=1).reshape(2 * NB, J * MODES)
    table = blade_table(NB)
    result = jnp.dot(table, reordered, precision=lax.Precision.HIGHEST, preferred_element_type=jnp.float32)
    return result.reshape(2, NB, J, MODES)
```

```python
import math

import jax
import jax.numpy as jnp
from jax import lax
from jax.sharding import PartitionSpec as P


def blade_table(blades, count):
    phases = jnp.arange(count, dtype=jnp.int32)
    target = jnp.arange(blades, dtype=jnp.int32)
    index = target[:, None] * phases[None, :] % blades
    theta = index.astype(jnp.float32) * (2.0 * math.pi / blades)
    cosine = jnp.cos(theta)
    sine = jnp.sin(theta)
    upper = jnp.concatenate([cosine, -sine], axis=1)
    lower = jnp.concatenate([sine, cosine], axis=1)
    return jnp.concatenate([upper, lower], axis=0) * (1.0 / math.sqrt(blades))


def shards(pressure, mode_shapes, point_weight, panel_order):
    weighted = mode_shapes * point_weight[None, :]
    phase_dev = pressure.shape[1]
    excite = pressure.shape[2]
    rows = pressure.reshape(2 * phase_dev * excite, pressure.shape[3])
    partial_forces = lax.dot_general(
        rows,
        lax.all_gather(weighted, "phase", axis=0, tiled=True),
        (((1,), (1,)), ((), ())),
        precision=lax.Precision.HIGHEST,
        preferred_element_type=jnp.float32,
    )
    row_count = partial_forces.shape[0]
    panel_count = panel_order.shape[0]
    panels = partial_forces.reshape(row_count, panel_count, -1)
    selector = (panel_order[:, None] == jnp.arange(panel_count, dtype=jnp.int32)[None, :]).astype(
        jnp.float32
    )
    reordered = jnp.einsum(
        "rqc,pq->rpc", panels, selector, precision=lax.Precision.HIGHEST
    ).reshape(row_count, -1)
    share = lax.psum_scatter(reordered, "slab", scatter_dimension=1, tiled=True)
    mode_local = share.shape[1]
    forces = share.reshape(2, phase_dev, excite, mode_local)
    blades = phase_dev * lax.axis_size("phase")
    gathered = lax.all_to_all(forces, "phase", split_axis=2, concat_axis=1, tiled=True)
    table = blade_table(blades, blades)
    result = jnp.dot(
        table,
        gathered.reshape(2 * blades, -1),
        precision=lax.Precision.HIGHEST,
        preferred_element_type=jnp.float32,
    )
    result = result.reshape(2, blades, -1, mode_local)
    return result


def solution(mesh):
    placed = (P(None, "phase", None, "slab"), P("phase", "slab"), P("slab"), P())
    return jax.shard_map(
        shards,
        mesh=mesh,
        in_specs=placed,
        out_specs=P(None, None, "phase", "slab"),
        check_vma=False,
    )
```

```python
import math

import jax
import jax.numpy as jnp
from jax import lax
from jax.sharding import Mesh
from jax.sharding import PartitionSpec as P

PHASE = ("px", "pz")
SLAB = ("sz", "sy", "sc")


def blade_table(blades, count):
    phases = jnp.arange(count, dtype=jnp.int32)
    target = jnp.arange(blades, dtype=jnp.int32)
    index = target[:, None] * phases[None, :] % blades
    theta = index.astype(jnp.float32) * (2.0 * math.pi / blades)
    cosine = jnp.cos(theta)
    sine = jnp.sin(theta)
    upper = jnp.concatenate([cosine, -sine], axis=1)
    lower = jnp.concatenate([sine, cosine], axis=1)
    return jnp.concatenate([upper, lower], axis=0) * (1.0 / math.sqrt(blades))


def ring_shift(value, axis, size, shift):
    return lax.ppermute(value, axis, [(s, (s + shift) % size) for s in range(size)])


def shards(pressure, mode_shapes, point_weight, panel_order):
    nx = lax.axis_size("px")
    xi = lax.axis_index("px")
    weighted = mode_shapes * point_weight[None, :]
    column_modes = lax.all_gather(weighted, "pz", axis=0, tiled=True)
    pressure_ring = jnp.stack(
        [pressure] + [ring_shift(pressure, "px", nx, d) for d in range(1, nx)], axis=1
    )
    two, _, phase_dev, excite, points = pressure_ring.shape
    rows = pressure_ring.reshape(two * nx * phase_dev * excite, points)
    partial = lax.dot_general(
        rows,
        column_modes,
        (((1,), (1,)), ((), ())),
        precision=lax.Precision.HIGHEST,
        preferred_element_type=jnp.float32,
    )
    column_width = partial.shape[1]
    partial = partial.reshape(two, nx, phase_dev, excite, column_width)
    pieces = [partial[:, 0]] + [
        ring_shift(partial[:, d], "px", nx, -d) for d in range(1, nx)
    ]
    own = jnp.stack(pieces, axis=3)
    row_count = two * phase_dev * excite
    panel_count = panel_order.shape[0]
    local_panels = panel_count // nx
    own = own.reshape(row_count, panel_count, -1)
    slot = jnp.arange(panel_count, dtype=jnp.int32)
    stored = ((xi + slot // local_panels) % nx) * local_panels + slot % local_panels
    selector = (panel_order[:, None] == stored[None, :]).astype(jnp.float32)
    reordered = jnp.einsum(
        "rqc,pq->rpc", own, selector, precision=lax.Precision.HIGHEST
    ).reshape(row_count, -1)
    slab_count = lax.axis_size(SLAB)
    keep_width = reordered.shape[1] // slab_count
    spread = reordered.reshape(row_count, slab_count, keep_width).transpose(1, 0, 2)
    share = lax.all_to_all(spread, SLAB, 0, 0, tiled=True).sum(axis=0)
    forces = share.reshape(two, phase_dev, excite, keep_width)
    blades = phase_dev * lax.axis_size(PHASE)
    gathered = lax.all_to_all(forces, PHASE, split_axis=2, concat_axis=1, tiled=True)
    table = blade_table(blades, blades)
    result = jnp.dot(
        table,
        gathered.reshape(2 * blades, -1),
        precision=lax.Precision.HIGHEST,
        preferred_element_type=jnp.float32,
    )
    return result.reshape(2, blades, -1, keep_width)


def solution(mesh):
    phase_n, slab_n = mesh.devices.shape
    torus = Mesh(mesh.devices.reshape(4, phase_n // 4, 4, slab_n // 8, 2), PHASE + SLAB)
    placed = (P(None, PHASE, None, SLAB), P(PHASE, SLAB), P(SLAB), P())
    return jax.shard_map(
        shards,
        mesh=torus,
        in_specs=placed,
        out_specs=P(None, None, PHASE, SLAB),
        check_vma=False,
    )
```

```python
import math

import jax
import jax.numpy as jnp
from jax import lax
from jax.sharding import Mesh
from jax.sharding import PartitionSpec as P

PHASE = ("px", "pz")
SLAB = ("sz", "sy", "sc")


def blade_table(blades, count):
    phases = jnp.arange(count, dtype=jnp.int32)
    target = jnp.arange(blades, dtype=jnp.int32)
    index = target[:, None] * phases[None, :] % blades
    theta = index.astype(jnp.float32) * (2.0 * math.pi / blades)
    cosine = jnp.cos(theta)
    sine = jnp.sin(theta)
    upper = jnp.concatenate([cosine, -sine], axis=1)
    lower = jnp.concatenate([sine, cosine], axis=1)
    return jnp.concatenate([upper, lower], axis=0) * (1.0 / math.sqrt(blades))


def ring_shift(value, axis, size, shift):
    return lax.ppermute(value, axis, [(s, (s + shift) % size) for s in range(size)])


def shards(pressure, mode_shapes, point_weight, panel_order):
    nx = lax.axis_size("px")
    xi = lax.axis_index("px")
    weighted = mode_shapes * point_weight[None, :]
    column_modes = lax.all_gather(weighted, "pz", axis=0, tiled=True)
    ring = [pressure] + [ring_shift(pressure, "px", nx, d) for d in range(1, nx)]
    two, phase_dev, excite, points = pressure.shape
    row_count = two * phase_dev * excite
    pieces = []
    for d, block in enumerate(ring):
        partial = lax.dot_general(
            block.reshape(row_count, points),
            column_modes,
            (((1,), (1,)), ((), ())),
            precision=lax.Precision.HIGHEST,
            preferred_element_type=jnp.float32,
        )
        pieces.append(partial if d == 0 else ring_shift(partial, "px", nx, -d))
    own = jnp.stack(pieces, axis=1)
    panel_count = panel_order.shape[0]
    local_panels = panel_count // nx
    own = own.reshape(row_count, panel_count, -1)
    slot = jnp.arange(panel_count, dtype=jnp.int32)
    stored = ((xi + slot // local_panels) % nx) * local_panels + slot % local_panels
    selector = (panel_order[:, None] == stored[None, :]).astype(jnp.float32)
    reordered = jnp.einsum(
        "rqc,pq->rpc", own, selector, precision=lax.Precision.HIGHEST
    ).reshape(row_count, -1)
    slab_count = lax.axis_size(SLAB)
    keep_width = reordered.shape[1] // slab_count
    blades = phase_dev * lax.axis_size(PHASE)
    table = blade_table(blades, blades)
    chains = 2
    lane = keep_width // chains
    spread = reordered.reshape(row_count, slab_count, chains, lane)
    outs = []
    for h in range(chains):
        part = spread[:, :, h].transpose(1, 0, 2)
        share = lax.all_to_all(part, SLAB, 0, 0, tiled=True).sum(axis=0)
        forces = share.reshape(two, phase_dev, excite, lane)
        gathered = lax.all_to_all(forces, PHASE, split_axis=2, concat_axis=1, tiled=True)
        result = jnp.dot(
            table,
            gathered.reshape(2 * blades, -1),
            precision=lax.Precision.HIGHEST,
            preferred_element_type=jnp.float32,
        )
        outs.append(result.reshape(2, blades, -1, lane))
    return jnp.concatenate(outs, axis=3)


def solution(mesh):
    phase_n, slab_n = mesh.devices.shape
    torus = Mesh(mesh.devices.reshape(4, phase_n // 4, 4, slab_n // 8, 2), PHASE + SLAB)
    placed = (P(None, PHASE, None, SLAB), P(PHASE, SLAB), P(SLAB), P())
    return jax.shard_map(
        shards,
        mesh=torus,
        in_specs=placed,
        out_specs=P(None, None, PHASE, SLAB),
        check_vma=False,
    )
```

```python
import math

import jax
import jax.numpy as jnp
from jax import lax
from jax.sharding import Mesh
from jax.sharding import PartitionSpec as P

PHASE = ("px", "pz")
SLAB = ("sz", "sy", "sc")


def blade_table(blades, count):
    phases = jnp.arange(count, dtype=jnp.int32)
    target = jnp.arange(blades, dtype=jnp.int32)
    index = target[:, None] * phases[None, :] % blades
    theta = index.astype(jnp.float32) * (2.0 * math.pi / blades)
    cosine = jnp.cos(theta)
    sine = jnp.sin(theta)
    upper = jnp.concatenate([cosine, -sine], axis=1)
    lower = jnp.concatenate([sine, cosine], axis=1)
    return jnp.concatenate([upper, lower], axis=0) * (1.0 / math.sqrt(blades))


def ring_shift(value, axis, size, shift):
    return lax.ppermute(value, axis, [(s, (s + shift) % size) for s in range(size)])


def shards(pressure, mode_shapes, point_weight, panel_order):
    nx = lax.axis_size("px")
    xi = lax.axis_index("px")
    weighted = mode_shapes * point_weight[None, :]
    column_modes = lax.all_gather(weighted, "pz", axis=0, tiled=True)
    ring = [pressure] + [ring_shift(pressure, "px", nx, d) for d in range(1, nx)]
    two, phase_dev, excite, points = pressure.shape
    row_count = two * phase_dev * excite
    pieces = []
    for d, block in enumerate(ring):
        partial = lax.dot_general(
            block.reshape(row_count, points),
            column_modes,
            (((1,), (1,)), ((), ())),
            precision=lax.Precision.HIGHEST,
            preferred_element_type=jnp.float32,
        )
        pieces.append(partial if d == 0 else ring_shift(partial, "px", nx, -d))
    own = jnp.stack(pieces, axis=1)
    panel_count = panel_order.shape[0]
    local_panels = panel_count // nx
    own = own.reshape(row_count, panel_count, -1)
    slot = jnp.arange(panel_count, dtype=jnp.int32)
    stored = ((xi + slot // local_panels) % nx) * local_panels + slot % local_panels
    selector = (panel_order[:, None] == stored[None, :]).astype(jnp.float32)
    reordered = jnp.einsum(
        "rqc,pq->rpc", own, selector, precision=lax.Precision.HIGHEST
    ).reshape(row_count, -1)
    slab_count = lax.axis_size(SLAB)
    keep_width = reordered.shape[1] // slab_count
    blades = phase_dev * lax.axis_size(PHASE)
    table = blade_table(blades, blades)
    spread = reordered.reshape(row_count, slab_count, keep_width).transpose(1, 0, 2)
    share = lax.all_to_all(spread, SLAB, 0, 0, tiled=True).sum(axis=0)
    forces = share.reshape(two, phase_dev, excite, keep_width)
    gathered = lax.all_to_all(forces, PHASE, split_axis=2, concat_axis=1, tiled=True)
    result = jnp.dot(
        table,
        gathered.reshape(2 * blades, -1),
        precision=lax.Precision.HIGHEST,
        preferred_element_type=jnp.float32,
    )
    return result.reshape(2, blades, -1, keep_width)


def solution(mesh):
    phase_n, slab_n = mesh.devices.shape
    torus = Mesh(mesh.devices.reshape(4, phase_n // 4, 4, slab_n // 8, 2), PHASE + SLAB)
    placed = (P(None, PHASE, None, SLAB), P(PHASE, SLAB), P(SLAB), P())
    return jax.shard_map(
        shards,
        mesh=torus,
        in_specs=placed,
        out_specs=P(None, None, PHASE, SLAB),
        check_vma=False,
    )
```

```python
import math

import jax
import jax.numpy as jnp
from jax import lax
from jax.sharding import Mesh
from jax.sharding import PartitionSpec as P

PHASE = ("px", "pz")
SLAB = ("sz", "sy", "sc")


def blade_table(blades, count):
    phases = jnp.arange(count, dtype=jnp.int32)
    target = jnp.arange(blades, dtype=jnp.int32)
    index = target[:, None] * phases[None, :] % blades
    theta = index.astype(jnp.float32) * (2.0 * math.pi / blades)
    cosine = jnp.cos(theta)
    sine = jnp.sin(theta)
    upper = jnp.concatenate([cosine, -sine], axis=1)
    lower = jnp.concatenate([sine, cosine], axis=1)
    return jnp.concatenate([upper, lower], axis=0) * (1.0 / math.sqrt(blades))


def ring_shift(value, axis, size, shift):
    return lax.ppermute(value, axis, [(s, (s + shift) % size) for s in range(size)])


def shards(pressure, mode_shapes, point_weight, panel_order):
    nx = lax.axis_size("px")
    xi = lax.axis_index("px")
    weighted = mode_shapes * point_weight[None, :]
    column_modes = lax.all_gather(weighted, "pz", axis=0, tiled=True)
    ring = [pressure] + [ring_shift(pressure, "px", nx, d) for d in range(1, nx)]
    two, phase_dev, excite, points = pressure.shape
    row_count = two * phase_dev * excite
    pieces = []
    for d, block in enumerate(ring):
        partial = lax.dot_general(
            block.reshape(row_count, points),
            column_modes,
            (((1,), (1,)), ((), ())),
            precision=lax.Precision.HIGH,
            preferred_element_type=jnp.float32,
        )
        pieces.append(partial if d == 0 else ring_shift(partial, "px", nx, -d))
    own = jnp.stack(pieces, axis=1)
    panel_count = panel_order.shape[0]
    local_panels = panel_count // nx
    own = own.reshape(row_count, panel_count, -1)
    slot = jnp.arange(panel_count, dtype=jnp.int32)
    stored = ((xi + slot // local_panels) % nx) * local_panels + slot % local_panels
    selector = (panel_order[:, None] == stored[None, :]).astype(jnp.float32)
    reordered = jnp.einsum(
        "rqc,pq->rpc", own, selector, precision=lax.Precision.HIGHEST
    ).reshape(row_count, -1)
    slab_count = lax.axis_size(SLAB)
    keep_width = reordered.shape[1] // slab_count
    blades = phase_dev * lax.axis_size(PHASE)
    table = blade_table(blades, blades)
    spread = reordered.reshape(row_count, slab_count, keep_width).transpose(1, 0, 2)
    share = lax.all_to_all(spread, SLAB, 0, 0, tiled=True).sum(axis=0)
    forces = share.reshape(two, phase_dev, excite, keep_width)
    gathered = lax.all_to_all(forces, PHASE, split_axis=2, concat_axis=1, tiled=True)
    result = jnp.dot(
        table,
        gathered.reshape(2 * blades, -1),
        precision=lax.Precision.HIGHEST,
        preferred_element_type=jnp.float32,
    )
    return result.reshape(2, blades, -1, keep_width)


def solution(mesh):
    phase_n, slab_n = mesh.devices.shape
    torus = Mesh(mesh.devices.reshape(4, phase_n // 4, 4, slab_n // 8, 2), PHASE + SLAB)
    placed = (P(None, PHASE, None, SLAB), P(PHASE, SLAB), P(SLAB), P())
    return jax.shard_map(
        shards,
        mesh=torus,
        in_specs=placed,
        out_specs=P(None, None, PHASE, SLAB),
        check_vma=False,
    )
```

```python
import math

import jax
import jax.numpy as jnp
from jax import lax
from jax.sharding import Mesh
from jax.sharding import PartitionSpec as P

PHASE = ("px", "pz")
SLAB = ("sz", "sy", "sc")


def blade_table(blades, count):
    phases = jnp.arange(count, dtype=jnp.int32)
    target = jnp.arange(blades, dtype=jnp.int32)
    index = target[:, None] * phases[None, :] % blades
    theta = index.astype(jnp.float32) * (2.0 * math.pi / blades)
    cosine = jnp.cos(theta)
    sine = jnp.sin(theta)
    upper = jnp.concatenate([cosine, -sine], axis=1)
    lower = jnp.concatenate([sine, cosine], axis=1)
    return jnp.concatenate([upper, lower], axis=0) * (1.0 / math.sqrt(blades))


def ring_shift(value, axis, size, shift):
    return lax.ppermute(value, axis, [(s, (s + shift) % size) for s in range(size)])


def shards(pressure, mode_shapes, point_weight, panel_order):
    nx = lax.axis_size("px")
    xi = lax.axis_index("px")
    weighted = mode_shapes * point_weight[None, :]
    column_modes = lax.all_gather(weighted, "pz", axis=0, tiled=True)
    ring = [pressure] + [ring_shift(pressure, "px", nx, d) for d in range(1, nx)]
    two, phase_dev, excite, points = pressure.shape
    row_count = two * phase_dev * excite
    pieces = []
    for d, block in enumerate(ring):
        partial = lax.dot_general(
            block.reshape(row_count, points),
            column_modes,
            (((1,), (1,)), ((), ())),
            precision=lax.Precision.HIGHEST,
            preferred_element_type=jnp.float32,
        )
        pieces.append(partial if d == 0 else ring_shift(partial, "px", nx, -d))
    own = jnp.stack(pieces, axis=1)
    panel_count = panel_order.shape[0]
    local_panels = panel_count // nx
    own = own.reshape(row_count, panel_count, -1)
    slot = jnp.arange(panel_count, dtype=jnp.int32)
    stored = ((xi + slot // local_panels) % nx) * local_panels + slot % local_panels
    selector = (panel_order[:, None] == stored[None, :]).astype(jnp.float32)
    reordered = jnp.einsum(
        "rqc,pq->rpc", own, selector, precision=lax.Precision.HIGHEST
    ).reshape(row_count, -1)
    slab_count = lax.axis_size(SLAB)
    keep_width = reordered.shape[1] // slab_count
    blades = phase_dev * lax.axis_size(PHASE)
    table = blade_table(blades, blades)
    cores = lax.axis_size("sc")
    ci = lax.axis_index("sc")
    spread = reordered.reshape(row_count, slab_count // cores, cores, keep_width)
    mine = jnp.take(spread, ci, axis=2)
    other = jnp.take(spread, 1 - ci, axis=2)
    paired = mine + lax.ppermute(other, "sc", [(0, 1), (1, 0)])
    share = lax.all_to_all(paired.transpose(1, 0, 2), ("sz", "sy"), 0, 0, tiled=True).sum(axis=0)
    forces = share.reshape(two, phase_dev, excite, keep_width)
    gathered = lax.all_to_all(forces, PHASE, split_axis=2, concat_axis=1, tiled=True)
    result = jnp.dot(
        table,
        gathered.reshape(2 * blades, -1),
        precision=lax.Precision.HIGHEST,
        preferred_element_type=jnp.float32,
    )
    return result.reshape(2, blades, -1, keep_width)


def solution(mesh):
    phase_n, slab_n = mesh.devices.shape
    torus = Mesh(mesh.devices.reshape(4, phase_n // 4, 4, slab_n // 8, 2), PHASE + SLAB)
    placed = (P(None, PHASE, None, SLAB), P(PHASE, SLAB), P(SLAB), P())
    return jax.shard_map(
        shards,
        mesh=torus,
        in_specs=placed,
        out_specs=P(None, None, PHASE, SLAB),
        check_vma=False,
    )
```

```python
import math

import jax
import jax.numpy as jnp
from jax import lax
from jax.sharding import Mesh
from jax.sharding import PartitionSpec as P

PHASE = ("px", "pz")
SLAB = ("sz", "sy", "sc")


def blade_table(blades, count):
    phases = jnp.arange(count, dtype=jnp.int32)
    target = jnp.arange(blades, dtype=jnp.int32)
    index = target[:, None] * phases[None, :] % blades
    theta = index.astype(jnp.float32) * (2.0 * math.pi / blades)
    cosine = jnp.cos(theta)
    sine = jnp.sin(theta)
    upper = jnp.concatenate([cosine, -sine], axis=1)
    lower = jnp.concatenate([sine, cosine], axis=1)
    return jnp.concatenate([upper, lower], axis=0) * (1.0 / math.sqrt(blades))


def ring_shift(value, axis, size, shift):
    return lax.ppermute(value, axis, [(s, (s + shift) % size) for s in range(size)])


def shards(pressure, mode_shapes, point_weight, panel_order):
    nx = lax.axis_size("px")
    xi = lax.axis_index("px")
    weighted = mode_shapes * point_weight[None, :]
    halves = 2
    half_rows = weighted.shape[0] // halves
    column_halves = [
        lax.all_gather(weighted[h * half_rows:(h + 1) * half_rows], "pz", axis=0, tiled=True)
        for h in range(halves)
    ]
    nz = lax.axis_size("pz")
    ring = [pressure] + [ring_shift(pressure, "px", nx, d) for d in range(1, nx)]
    two, phase_dev, excite, points = pressure.shape
    row_count = two * phase_dev * excite
    pieces = []
    for d, block in enumerate(ring):
        partial = jnp.stack(
            [
                lax.dot_general(
                    block.reshape(row_count, points),
                    column_half,
                    (((1,), (1,)), ((), ())),
                    precision=lax.Precision.HIGHEST,
                    preferred_element_type=jnp.float32,
                ).reshape(row_count, nz, half_rows)
                for column_half in column_halves
            ],
            axis=2,
        ).reshape(row_count, -1)
        pieces.append(partial if d == 0 else ring_shift(partial, "px", nx, -d))
    own = jnp.stack(pieces, axis=1)
    panel_count = panel_order.shape[0]
    local_panels = panel_count // nx
    own = own.reshape(row_count, panel_count, -1)
    slot = jnp.arange(panel_count, dtype=jnp.int32)
    stored = ((xi + slot // local_panels) % nx) * local_panels + slot % local_panels
    selector = (panel_order[:, None] == stored[None, :]).astype(jnp.float32)
    reordered = jnp.einsum(
        "rqc,pq->rpc", own, selector, precision=lax.Precision.HIGHEST
    ).reshape(row_count, -1)
    slab_count = lax.axis_size(SLAB)
    keep_width = reordered.shape[1] // slab_count
    blades = phase_dev * lax.axis_size(PHASE)
    table = blade_table(blades, blades)
    cores = lax.axis_size("sc")
    ci = lax.axis_index("sc")
    spread = reordered.reshape(row_count, slab_count // cores, cores, keep_width)
    mine = jnp.take(spread, ci, axis=2)
    other = jnp.take(spread, 1 - ci, axis=2)
    paired = mine + lax.ppermute(other, "sc", [(0, 1), (1, 0)])
    share = lax.all_to_all(paired.transpose(1, 0, 2), ("sz", "sy"), 0, 0, tiled=True).sum(axis=0)
    forces = share.reshape(two, phase_dev, excite, keep_width)
    gathered = lax.all_to_all(forces, PHASE, split_axis=2, concat_axis=1, tiled=True)
    result = jnp.dot(
        table,
        gathered.reshape(2 * blades, -1),
        precision=lax.Precision.HIGHEST,
        preferred_element_type=jnp.float32,
    )
    return result.reshape(2, blades, -1, keep_width)


def solution(mesh):
    phase_n, slab_n = mesh.devices.shape
    torus = Mesh(mesh.devices.reshape(4, phase_n // 4, 4, slab_n // 8, 2), PHASE + SLAB)
    placed = (P(None, PHASE, None, SLAB), P(PHASE, SLAB), P(SLAB), P())
    return jax.shard_map(
        shards,
        mesh=torus,
        in_specs=placed,
        out_specs=P(None, None, PHASE, SLAB),
        check_vma=False,
    )
```

```python
import math

import jax
import jax.numpy as jnp
from jax import lax
from jax.sharding import Mesh
from jax.sharding import PartitionSpec as P

PHASE = ("px", "pz")
SLAB = ("sz", "sy", "sc")


def blade_table(blades, count):
    phases = jnp.arange(count, dtype=jnp.int32)
    target = jnp.arange(blades, dtype=jnp.int32)
    index = target[:, None] * phases[None, :] % blades
    theta = index.astype(jnp.float32) * (2.0 * math.pi / blades)
    cosine = jnp.cos(theta)
    sine = jnp.sin(theta)
    upper = jnp.concatenate([cosine, -sine], axis=1)
    lower = jnp.concatenate([sine, cosine], axis=1)
    return jnp.concatenate([upper, lower], axis=0) * (1.0 / math.sqrt(blades))


def ring_shift(value, axis, size, shift):
    return lax.ppermute(value, axis, [(s, (s + shift) % size) for s in range(size)])


def shards(pressure, mode_shapes, point_weight, panel_order):
    nx = lax.axis_size("px")
    xi = lax.axis_index("px")
    column_modes = lax.all_gather(mode_shapes, "pz", axis=0, tiled=True)
    weighted = pressure * point_weight
    ring = [weighted] + [ring_shift(weighted, "px", nx, d) for d in range(1, nx)]
    two, phase_dev, excite, points = pressure.shape
    row_count = two * phase_dev * excite
    pieces = []
    for d, block in enumerate(ring):
        partial = lax.dot_general(
            block.reshape(row_count, points),
            column_modes,
            (((1,), (1,)), ((), ())),
            precision=lax.Precision.HIGHEST,
            preferred_element_type=jnp.float32,
        )
        pieces.append(partial if d == 0 else ring_shift(partial, "px", nx, -d))
    own = jnp.stack(pieces, axis=1)
    panel_count = panel_order.shape[0]
    local_panels = panel_count // nx
    own = own.reshape(row_count, panel_count, -1)
    slot = jnp.arange(panel_count, dtype=jnp.int32)
    stored = ((xi + slot // local_panels) % nx) * local_panels + slot % local_panels
    selector = (panel_order[:, None] == stored[None, :]).astype(jnp.float32)
    reordered = jnp.einsum(
        "rqc,pq->rpc", own, selector, precision=lax.Precision.HIGHEST
    ).reshape(row_count, -1)
    slab_count = lax.axis_size(SLAB)
    keep_width = reordered.shape[1] // slab_count
    blades = phase_dev * lax.axis_size(PHASE)
    table = blade_table(blades, blades)
    cores = lax.axis_size("sc")
    ci = lax.axis_index("sc")
    spread = reordered.reshape(row_count, slab_count // cores, cores, keep_width)
    mine = jnp.take(spread, ci, axis=2)
    other = jnp.take(spread, 1 - ci, axis=2)
    paired = mine + lax.ppermute(other, "sc", [(0, 1), (1, 0)])
    share = lax.all_to_all(paired.transpose(1, 0, 2), ("sz", "sy"), 0, 0, tiled=True).sum(axis=0)
    forces = share.reshape(two, phase_dev, excite, keep_width)
    gathered = lax.all_to_all(forces, PHASE, split_axis=2, concat_axis=1, tiled=True)
    result = jnp.dot(
        table,
        gathered.reshape(2 * blades, -1),
        precision=lax.Precision.HIGHEST,
        preferred_element_type=jnp.float32,
    )
    return result.reshape(2, blades, -1, keep_width)


def solution(mesh):
    phase_n, slab_n = mesh.devices.shape
    torus = Mesh(mesh.devices.reshape(4, phase_n // 4, 4, slab_n // 8, 2), PHASE + SLAB)
    placed = (P(None, PHASE, None, SLAB), P(PHASE, SLAB), P(SLAB), P())
    return jax.shard_map(
        shards,
        mesh=torus,
        in_specs=placed,
        out_specs=P(None, None, PHASE, SLAB),
        check_vma=False,
    )
```

```python
import math

import jax
import jax.numpy as jnp
from jax import lax
from jax.sharding import Mesh
from jax.sharding import PartitionSpec as P

PHASE = ("px", "pz")
SLAB = ("sz", "sy", "sc")


def blade_table(blades, count):
    phases = jnp.arange(count, dtype=jnp.int32)
    target = jnp.arange(blades, dtype=jnp.int32)
    index = target[:, None] * phases[None, :] % blades
    theta = index.astype(jnp.float32) * (2.0 * math.pi / blades)
    cosine = jnp.cos(theta)
    sine = jnp.sin(theta)
    upper = jnp.concatenate([cosine, -sine], axis=1)
    lower = jnp.concatenate([sine, cosine], axis=1)
    return jnp.concatenate([upper, lower], axis=0) * (1.0 / math.sqrt(blades))


def ring_shift(value, axis, size, shift):
    return lax.ppermute(value, axis, [(s, (s + shift) % size) for s in range(size)])


def shards(pressure, mode_shapes, point_weight, panel_order):
    nx = lax.axis_size("px")
    xi = lax.axis_index("px")
    weighted = mode_shapes * point_weight[None, :]
    column_modes = lax.all_gather(weighted, "pz", axis=0, tiled=True)
    ring = [pressure] + [ring_shift(pressure, "px", nx, d) for d in range(1, nx)]
    two, phase_dev, excite, points = pressure.shape
    row_count = two * phase_dev * excite
    pieces = []
    for d, block in enumerate(ring):
        partial = lax.dot_general(
            block.reshape(row_count, points),
            column_modes,
            (((1,), (1,)), ((), ())),
            precision=lax.Precision.HIGHEST,
            preferred_element_type=jnp.float32,
        )
        pieces.append(partial)
    by_owner = jnp.take(jnp.stack(pieces), (xi - jnp.arange(nx)) % nx, axis=0)
    own = lax.all_to_all(by_owner, "px", 0, 0, tiled=True).transpose(1, 0, 2)
    panel_count = panel_order.shape[0]
    own = own.reshape(row_count, panel_count, -1)
    stored = jnp.arange(panel_count, dtype=jnp.int32)
    selector = (panel_order[:, None] == stored[None, :]).astype(jnp.float32)
    reordered = jnp.einsum(
        "rqc,pq->rpc", own, selector, precision=lax.Precision.HIGHEST
    ).reshape(row_count, -1)
    slab_count = lax.axis_size(SLAB)
    keep_width = reordered.shape[1] // slab_count
    blades = phase_dev * lax.axis_size(PHASE)
    table = blade_table(blades, blades)
    cores = lax.axis_size("sc")
    ci = lax.axis_index("sc")
    spread = reordered.reshape(row_count, slab_count // cores, cores, keep_width)
    mine = jnp.take(spread, ci, axis=2)
    other = jnp.take(spread, 1 - ci, axis=2)
    paired = mine + lax.ppermute(other, "sc", [(0, 1), (1, 0)])
    share = lax.all_to_all(paired.transpose(1, 0, 2), ("sz", "sy"), 0, 0, tiled=True).sum(axis=0)
    forces = share.reshape(two, phase_dev, excite, keep_width)
    gathered = lax.all_to_all(forces, PHASE, split_axis=2, concat_axis=1, tiled=True)
    result = jnp.dot(
        table,
        gathered.reshape(2 * blades, -1),
        precision=lax.Precision.HIGHEST,
        preferred_element_type=jnp.float32,
    )
    return result.reshape(2, blades, -1, keep_width)


def solution(mesh):
    phase_n, slab_n = mesh.devices.shape
    torus = Mesh(mesh.devices.reshape(4, phase_n // 4, 4, slab_n // 8, 2), PHASE + SLAB)
    placed = (P(None, PHASE, None, SLAB), P(PHASE, SLAB), P(SLAB), P())
    return jax.shard_map(
        shards,
        mesh=torus,
        in_specs=placed,
        out_specs=P(None, None, PHASE, SLAB),
        check_vma=False,
    )
```
